128 devices in a mesh: shard: 8 (over y, core), tensor: 4 (over z), section: 4 (over x).
Axes of the slice: x: 4, y: 4, z: 4, core: 2. Of those that a mesh axis runs over, the one named last changes fastest.
Arguments:
- activations: bfloat16 [4, 16384, 2048], P('section', 'shard'), may hold values from -500 to 500, as said below
- out_grad: bfloat16 [4, 16384, 8192], P('section', 'shard', 'tensor'), may hold values from -30 to 30, as said below
- basis: float32 [4, 2048, 256], P('section', 'shard'), may hold values from -0.125 to 0.125
- first_moment: float32 [4, 256, 8192], P('section', 'shard', 'tensor'), may hold values from -6 to 6
- second_moment: float32 [4, 256, 8192], P('section', 'shard', 'tensor'), may hold values from 0.5 to 2
- gain_partial: float32 [4, 8, 2048], P('section', 'shard'), may hold values from -4096 to 4096
- gain_first: float32 [4, 2048], P('section', 'shard'), may hold values from -6 to 6
- gain_second: float32 [4, 2048], P('section', 'shard'), may hold values from 0.5 to 2
Outputs:
- update: float32 [4, 2048, 8192], P('section', 'shard', 'tensor')
- first_out: float32 [4, 256, 8192], P('section', 'shard', 'tensor')
- second_out: float32 [4, 256, 8192], P('section', 'shard', 'tensor')
- new_basis: float32 [4, 2048, 256], P('section', ('shard', 'tensor'))
- gain_step: float32 [4, 2048], P('section', 'shard')
- gain_first_out: float32 [4, 2048], P('section', 'shard')
- gain_second_out: float32 [4, 2048], P('section', 'shard')
The draws below stay inside these ranges and needn't reach their ends.
Inputs may be any that keep to these rules, and one draw needn't show every extreme that they name: Real-valued activations whose column scales differ from column to column. `out_grad`: Real-valued gradients whose column scales differ from column to column.
All inputs are finite; a program needn't handle non-finite values.
Results may differ from the reference program's by a relative error of at most 0.0003.
Values sent between devices are 32-bit elements; how exact they have to be, the bound alone decides.
No kernel may reach another device: no remote copies, remote signals or barrier semaphores. Data moves between devices by JAX's collectives and lax.ppermute only.
A program may use at most 128 MiB of HBM per device.

```python
import math
import jax
import jax.numpy as jnp
from jax import lax

D = 2048
FF = 8192
RANK = 256
TOK_DEV = 2048
NS_STEPS = 5
STEP = 8
LAYERS = 4
TOKENS = 16384
N_SHARD = 8


def draw_activations(key, part):
    key_values, key_columns = jax.random.split(key, 2)
    column_pos = jnp.arange(D, dtype=jnp.float32) / float(D)
    layer_pos = jnp.arange(LAYERS, dtype=jnp.float32) / float(max(LAYERS - 1, 1))
    random_scale = jnp.exp(jax.random.uniform(key_columns, (LAYERS, 1, D), jnp.float32) * math.log(10.0))
    rising = jnp.exp(1.1 * column_pos)
    column_scale = random_scale * rising[None, None, :] * jnp.exp(0.3 * layer_pos)[:, None, None]
    values = jnp.clip(jax.random.normal(key_values, (LAYERS, TOKENS, D), jnp.float32), -4.0, 4.0)
    return (values * column_scale).astype(jnp.bfloat16)


def draw_out_grad(key, part):
    key_values = jax.random.fold_in(key, 17)
    column_pos = jnp.arange(FF, dtype=jnp.float32) / float(FF)
    rising = jnp.exp(1.1 * column_pos)
    values = jnp.clip(jax.random.normal(key_values, (LAYERS, TOKENS, FF), jnp.float32), -5.0, 5.0)
    return (values * rising[None, None, :]).astype(jnp.bfloat16)


def levels(rng, shape, pieces, smallest, largest):
    def one(axis_at, shards_of):
        heights = jax.random.uniform(jax.random.fold_in(jax.random.fold_in(rng, 6), axis_at), (shards_of,), jnp.float32, smallest / len(pieces), largest / len(pieces))
        return jnp.repeat(jnp.exp(heights), shape[axis_at] // shards_of).reshape((-1,) + (1,) * (len(shape) - axis_at - 1))

    factor_of = one(*pieces[0])
    for cut in pieces[1:]:
        factor_of = factor_of * one(*cut)
    return factor_of


def scatter_about(own_key, extent, spread, limit, cuts=(), kind=jnp.bfloat16):
    array = jax.random.normal(own_key, extent, jnp.float32) * spread
    if len(cuts) > 0:
        array = levels(own_key, extent, cuts, -0.22, 0.18) * array
    return jnp.clip(array, min=-limit, max=limit).astype(kind)


def setup_inputs(seed: int = 0) -> dict:
    arg_keys = jax.random.split(jax.random.key(seed), 9)
    activations = draw_activations(jax.random.fold_in(arg_keys[8], 71), 0)
    out_grad = draw_out_grad(jax.random.fold_in(arg_keys[8], 71), 0)
    basis = scatter_about(arg_keys[2], (LAYERS, D, RANK), D ** -0.5, 0.125, ((0, 4), (1, 8)), jnp.float32)
    first_moment = scatter_about(arg_keys[3], (LAYERS, RANK, FF), 1.0, 6.0, ((0, 4), (1, 8), (2, 4)), jnp.float32)
    second_moment = jnp.clip(jnp.exp(math.log(2.0) - 1.3862944 * jax.random.uniform(arg_keys[4], (LAYERS, RANK, FF), jnp.float32) ** levels(arg_keys[4], (LAYERS, RANK, FF), ((0, 4), (1, 8), (2, 4)), -0.2, 0.2)), 0.5, 2.0)
    gain_partial = scatter_about(arg_keys[5], (LAYERS, N_SHARD, D), 700.0, 4096.0, ((0, 4), (1, 8)), jnp.float32)
    gain_first = scatter_about(arg_keys[6], (LAYERS, D), 1.0, 6.0, ((0, 4), (1, 8)), jnp.float32)
    gain_second = jnp.clip(jnp.exp(math.log(2.0) - 1.3862944 * jax.random.uniform(arg_keys[7], (LAYERS, D), jnp.float32) ** levels(arg_keys[7], (LAYERS, D), ((0, 4), (1, 8)), -0.2, 0.2)), 0.5, 2.0)
    return {"activations": activations, "out_grad": out_grad, "basis": basis, "first_moment": first_moment, "second_moment": second_moment, "gain_partial": gain_partial, "gain_first": gain_first, "gain_second": gain_second}


exact_mode = lax.Precision.HIGHEST
beta_one = 0.9
beta_two = 0.999
adam_eps = 1e-08
clip_eps = 1e-06
ns_eps = 1e-07
coef_first = 3.4445
coef_second = -4.775
coef_third = 2.0315

def summed_gradient(tokens_in, grads_out):
    token_blocks = tokens_in.reshape(N_SHARD, TOK_DEV, D)
    grad_blocks = grads_out.reshape(N_SHARD, TOK_DEV, FF)

    def accumulate(total, pair):
        partial_grad = jnp.dot(pair[0].T, pair[1], preferred_element_type=jnp.float32)
        return (total + partial_grad, None)
    total, unused = lax.scan(accumulate, jnp.zeros((D, FF), jnp.float32), (token_blocks, grad_blocks))
    return total

def adam_direction(clipped, first_old, second_old):
    first_new = beta_one * first_old + (1.0 - beta_one) * clipped
    second_new = beta_two * second_old + (1.0 - beta_two) * clipped * clipped
    direction = first_new / (1.0 - beta_one ** STEP) / (jnp.sqrt(second_new / (1.0 - beta_two ** STEP)) + adam_eps)
    return (first_new, second_new, direction)

def orthogonalize(refreshed):
    current = refreshed / jnp.sqrt(jnp.sum(refreshed * refreshed) + ns_eps)
    for step_index in range(NS_STEPS):
        gram = jnp.dot(current.T, current, precision=exact_mode)
        mixer = coef_second * gram + coef_third * jnp.dot(gram, gram, precision=exact_mode)
        current = coef_first * current + jnp.dot(current, mixer, precision=exact_mode)
    return current

def reference(activations, out_grad, basis, first_moment, second_moment, gain_partial, gain_first, gain_second):
    grads = []
    square_sum = jnp.zeros((), jnp.float32)
    for layer_index in range(LAYERS):
        grad_layer = summed_gradient(activations[layer_index], out_grad[layer_index])
        grads.append(grad_layer)
        square_sum = square_sum + jnp.sum(grad_layer * grad_layer)
    gain_total = lax.optimization_barrier(jnp.sum(gain_partial, axis=1))
    square_sum = square_sum + jnp.sum(gain_total * gain_total)
    mean_sq = square_sum / float(LAYERS * (D * FF + D))
    clip = jnp.minimum(1.0, lax.rsqrt(mean_sq + clip_eps))
    updates = []
    firsts = []
    seconds = []
    bases = []
    for layer_index in range(LAYERS):
        proj = jnp.dot(basis[layer_index].T, grads[layer_index], precision=exact_mode)
        first_new, second_new, direction = adam_direction(clip * proj, first_moment[layer_index], second_moment[layer_index])
        updates.append(jnp.dot(basis[layer_index], direction, precision=exact_mode))
        firsts.append(first_new)
        seconds.append(second_new)
        refreshed = jnp.dot(grads[layer_index], proj.T, precision=exact_mode)
        bases.append(orthogonalize(refreshed))
    gain_first_new, gain_second_new, gain_dir = adam_direction(clip * gain_total, gain_first, gain_second)
    return (jnp.stack(updates), jnp.stack(firsts), jnp.stack(seconds), jnp.stack(bases), gain_dir, gain_first_new, gain_second_new)
```

```python
import jax
import jax.numpy as jnp
from jax import lax
from jax.sharding import PartitionSpec as P

D = 2048
FF = 8192
NS_STEPS = 5
STEP = 8


exact_mode = lax.Precision.HIGHEST
beta_one = 0.9
beta_two = 0.999
adam_eps = 1e-08
clip_eps = 1e-06
ns_eps = 1e-07
coef_first = 3.4445
coef_second = -4.775
coef_third = 2.0315
PAD = 8


def adam_direction(clipped, first_old, second_old):
    first_new = beta_one * first_old + (1.0 - beta_one) * clipped
    second_new = beta_two * second_old + (1.0 - beta_two) * clipped * clipped
    direction = (
        first_new
        / (1.0 - beta_one**STEP)
        / (jnp.sqrt(second_new / (1.0 - beta_two**STEP)) + adam_eps)
    )
    return (first_new, second_new, direction)


def mixer_of(current):
    gram = jnp.dot(current.T, current, precision=exact_mode)
    return coef_second * gram + coef_third * jnp.dot(gram, gram, precision=exact_mode)


def shards(
    activations, out_grad, basis, first_moment, second_moment, gain_partial, gain_first, gain_second
):
    tensors = lax.axis_size("tensor")
    shard_pos = lax.axis_index("shard")
    tensor_pos = lax.axis_index("tensor")
    layer_count = activations.shape[0]
    rows_here = basis.shape[1]
    rank_rows = first_moment.shape[1]
    cols_here = out_grad.shape[2]
    rank = basis.shape[2]
    out_rows = rows_here // tensors
    layer_index = 0
    tokens_in = activations[layer_index]
    grads_out = out_grad[layer_index]
    basis_here = basis[layer_index]

    partial_grad = lax.dot_general(
        tokens_in, grads_out, (((0,), (0,)), ((), ())), preferred_element_type=jnp.float32
    )
    grad_block = lax.psum_scatter(partial_grad, "shard", scatter_dimension=0, tiled=True)
    part_proj = jnp.dot(basis_here.T, grad_block, precision=exact_mode)
    square_part = jnp.sum(grad_block * grad_block)

    gain_row = gain_partial[layer_index, 0]
    gain_len = gain_row.shape[0]
    gain_rows = -(-gain_len // cols_here)
    gain_block = jnp.pad(gain_row, (0, gain_rows * cols_here - gain_len)).reshape(gain_rows, cols_here)
    extra = jnp.zeros((PAD, cols_here), jnp.float32).at[0, 0].set(square_part)
    packed = lax.psum(jnp.concatenate([part_proj, gain_block, extra], axis=0), "shard")
    proj_full = packed[:rank]
    gain_total = packed[rank:rank + gain_rows].reshape(-1)[:gain_len]
    square_shard = packed[rank + gain_rows, 0]
    proj_rows = lax.dynamic_slice_in_dim(proj_full, shard_pos * rank_rows, rank_rows, 0)

    refresh_part = lax.dot_general(
        grad_block, proj_full, (((1,), (1,)), ((), ())), precision=exact_mode
    )
    extra_r = jnp.zeros((PAD, rank), jnp.float32).at[1, 0].set(square_shard)
    packed_r = lax.psum(jnp.concatenate([refresh_part, extra_r], axis=0), "tensor")
    refresh_rows = packed_r[:rows_here]
    square_st = packed_r[rows_here + 1, 0]
    refreshed = lax.all_gather(refresh_rows, "shard", axis=0, tiled=True)

    gain_own = lax.dynamic_slice_in_dim(gain_total, shard_pos * rows_here, rows_here, 0)
    square_local = square_st + jnp.sum(gain_total * gain_total)
    total_sq = lax.psum(square_local, "section")
    entry_count = float(lax.axis_size("section") * layer_count * (D * FF + D))
    clip = jnp.minimum(1.0, lax.rsqrt(total_sq / entry_count + clip_eps))

    first_new, second_new, direction = adam_direction(
        clip * proj_rows, first_moment[layer_index], second_moment[layer_index]
    )
    update_here = jnp.dot(
        basis_here, lax.all_gather(direction, "shard", axis=0, tiled=True), precision=exact_mode
    )

    current = refreshed / jnp.sqrt(jnp.sum(refreshed * refreshed) + ns_eps)
    for step_index in range(NS_STEPS - 1):
        current = coef_first * current + jnp.dot(current, mixer_of(current), precision=exact_mode)
    row_start = shard_pos * rows_here + tensor_pos * out_rows
    own = lax.dynamic_slice_in_dim(current, row_start, out_rows, 0)
    own = coef_first * own + jnp.dot(own, mixer_of(current), precision=exact_mode)

    gain_first_new, gain_second_new, gain_dir = adam_direction(
        clip * gain_own, gain_first[layer_index], gain_second[layer_index]
    )
    return (
        update_here[None],
        first_new[None],
        second_new[None],
        own[None],
        gain_dir[None],
        gain_first_new[None],
        gain_second_new[None],
    )


def solution(mesh):
    placed = (
        P("section", "shard", None),
        P("section", "shard", "tensor"),
        P("section", "shard", None),
        P("section", "shard", "tensor"),
        P("section", "shard", "tensor"),
        P("section", "shard", None),
        P("section", "shard"),
        P("section", "shard"),
    )
    return jax.shard_map(
        shards,
        mesh=mesh,
        in_specs=placed,
        out_specs=(
            P("section", "shard", "tensor"),
            P("section", "shard", "tensor"),
            P("section", "shard", "tensor"),
            P("section", ("shard", "tensor"), None),
            P("section", "shard"),
            P("section", "shard"),
            P("section", "shard"),
        ),
        check_vma=False,
    )
```

```python
import jax
import jax.numpy as jnp
from jax import lax
from jax.sharding import PartitionSpec as P

D = 2048
FF = 8192
NS_STEPS = 5
STEP = 8


exact_mode = lax.Precision.HIGHEST
beta_one = 0.9
beta_two = 0.999
adam_eps = 1e-08
clip_eps = 1e-06
ns_eps = 1e-07
coef_first = 3.4445
coef_second = -4.775
coef_third = 2.0315
PAD = 8


def adam_direction(clipped, first_old, second_old):
    first_new = beta_one * first_old + (1.0 - beta_one) * clipped
    second_new = beta_two * second_old + (1.0 - beta_two) * clipped * clipped
    direction = (
        first_new
        / (1.0 - beta_one**STEP)
        / (jnp.sqrt(second_new / (1.0 - beta_two**STEP)) + adam_eps)
    )
    return (first_new, second_new, direction)


def mixer_of(current):
    gram = jnp.dot(current.T, current, precision=exact_mode)
    return coef_second * gram + coef_third * jnp.dot(gram, gram, precision=exact_mode)


def split3(x):
    hi = lax.reduce_precision(x, exponent_bits=8, mantissa_bits=7)
    rest = x - hi
    mid = lax.reduce_precision(rest, exponent_bits=8, mantissa_bits=7)
    lo = rest - mid
    return tuple(p.astype(jnp.bfloat16) for p in (hi, mid, lo))


def dot_split(lhs, rhs_pieces, dims):
    out = None
    for piece in rhs_pieces:
        term = lax.dot_general(lhs, piece, dims, preferred_element_type=jnp.float32)
        out = term if out is None else out + term
    return out


def butterfly_sum(x, axis):
    n = lax.axis_size(axis)
    k = 1
    while k < n:
        x = x + lax.ppermute(x, axis, [(i, i ^ k) for i in range(n)])
        k *= 2
    return x


def shards(
    activations, out_grad, basis, first_moment, second_moment, gain_partial, gain_first, gain_second
):
    tensors = lax.axis_size("tensor")
    shard_count = lax.axis_size("shard")
    shard_pos = lax.axis_index("shard")
    tensor_pos = lax.axis_index("tensor")
    layer_count = activations.shape[0]
    rows_here = basis.shape[1]
    rank_rows = first_moment.shape[1]
    cols_here = out_grad.shape[2]
    rank = basis.shape[2]
    out_rows = rows_here // tensors
    layer_index = 0
    tokens_in = activations[layer_index]
    grads_out = out_grad[layer_index]
    basis_here = basis[layer_index]

    partial_grad = lax.dot_general(
        tokens_in, grads_out, (((0,), (0,)), ((), ())), preferred_element_type=jnp.float32
    )
    grad_block = lax.psum_scatter(partial_grad, "shard", scatter_dimension=0, tiled=True)

    basis_full = lax.all_gather(basis_here, "shard", axis=0, tiled=True)
    token_basis = dot_split(tokens_in, split3(basis_full), (((1,), (0,)), ((), ())))
    part_proj = dot_split(grads_out, split3(token_basis), (((0,), (0,)), ((), ()))).T
    gain_row = gain_partial[layer_index, 0]
    gain_len = gain_row.shape[0]
    gain_rows = -(-gain_len // cols_here)
    gain_block = jnp.pad(gain_row, (0, gain_rows * cols_here - gain_len)).reshape(gain_rows, cols_here)
    extra = jnp.zeros((PAD - gain_rows % PAD, cols_here), jnp.float32)
    packed = butterfly_sum(jnp.concatenate([part_proj, gain_block, extra], axis=0), "shard")
    proj_full = packed[:rank]
    gain_total = packed[rank:rank + gain_rows].reshape(-1)[:gain_len]
    proj_rows = lax.dynamic_slice_in_dim(proj_full, shard_pos * rank_rows, rank_rows, 0)

    square_part = jnp.sum(grad_block * grad_block)
    refresh_part = lax.dot_general(
        grad_block, proj_full, (((1,), (1,)), ((), ())), precision=exact_mode
    )
    extra_r = jnp.zeros((PAD, rank), jnp.float32).at[0, 0].set(square_part)
    packed_r = butterfly_sum(jnp.concatenate([refresh_part, extra_r], axis=0), "tensor")
    gathered = lax.all_gather(packed_r, "shard", axis=0, tiled=False)
    refreshed = gathered[:, :rows_here].reshape(shard_count * rows_here, rank)
    square_st = jnp.sum(gathered[:, rows_here, 0])

    gain_own = lax.dynamic_slice_in_dim(gain_total, shard_pos * rows_here, rows_here, 0)
    square_local = square_st + jnp.sum(gain_total * gain_total)
    total_sq = lax.psum(square_local, "section")
    entry_count = float(lax.axis_size("section") * layer_count * (D * FF + D))
    clip = jnp.minimum(1.0, lax.rsqrt(total_sq / entry_count + clip_eps))

    first_new, second_new, direction = adam_direction(
        clip * proj_rows, first_moment[layer_index], second_moment[layer_index]
    )
    update_here = jnp.dot(
        basis_here, lax.all_gather(direction, "shard", axis=0, tiled=True), precision=exact_mode
    )

    current = refreshed / jnp.sqrt(jnp.sum(refreshed * refreshed) + ns_eps)
    for step_index in range(NS_STEPS - 1):
        current = coef_first * current + jnp.dot(current, mixer_of(current), precision=exact_mode)
    row_start = shard_pos * rows_here + tensor_pos * out_rows
    own = lax.dynamic_slice_in_dim(current, row_start, out_rows, 0)
    own = coef_first * own + jnp.dot(own, mixer_of(current), precision=exact_mode)

    gain_first_new, gain_second_new, gain_dir = adam_direction(
        clip * gain_own, gain_first[layer_index], gain_second[layer_index]
    )
    return (
        update_here[None],
        first_new[None],
        second_new[None],
        own[None],
        gain_dir[None],
        gain_first_new[None],
        gain_second_new[None],
    )


def solution(mesh):
    placed = (
        P("section", "shard", None),
        P("section", "shard", "tensor"),
        P("section", "shard", None),
        P("section", "shard", "tensor"),
        P("section", "shard", "tensor"),
        P("section", "shard", None),
        P("section", "shard"),
        P("section", "shard"),
    )
    return jax.shard_map(
        shards,
        mesh=mesh,
        in_specs=placed,
        out_specs=(
            P("section", "shard", "tensor"),
            P("section", "shard", "tensor"),
            P("section", "shard", "tensor"),
            P("section", ("shard", "tensor"), None),
            P("section", "shard"),
            P("section", "shard"),
            P("section", "shard"),
        ),
        check_vma=False,
    )
```

```python
import jax
import jax.numpy as jnp
from jax import lax
from jax.sharding import PartitionSpec as P

D = 2048
FF = 8192
NS_STEPS = 5
STEP = 8


exact_mode = lax.Precision.HIGHEST
beta_one = 0.9
beta_two = 0.999
adam_eps = 1e-08
clip_eps = 1e-06
ns_eps = 1e-07
coef_first = 3.4445
coef_second = -4.775
coef_third = 2.0315
PAD = 8


def adam_direction(clipped, first_old, second_old):
    first_new = beta_one * first_old + (1.0 - beta_one) * clipped
    second_new = beta_two * second_old + (1.0 - beta_two) * clipped * clipped
    direction = (
        first_new
        / (1.0 - beta_one**STEP)
        / (jnp.sqrt(second_new / (1.0 - beta_two**STEP)) + adam_eps)
    )
    return (first_new, second_new, direction)


def mixer_of(current):
    gram = jnp.dot(current.T, current, precision=exact_mode)
    return coef_second * gram + coef_third * jnp.dot(gram, gram, precision=exact_mode)


def split3(x):
    hi = lax.reduce_precision(x, exponent_bits=8, mantissa_bits=7)
    rest = x - hi
    mid = lax.reduce_precision(rest, exponent_bits=8, mantissa_bits=7)
    lo = rest - mid
    return tuple(p.astype(jnp.bfloat16) for p in (hi, mid, lo))


def dot_split(lhs, rhs_pieces, dims):
    out = None
    for piece in rhs_pieces:
        term = lax.dot_general(lhs, piece, dims, preferred_element_type=jnp.float32)
        out = term if out is None else out + term
    return out


def butterfly_sum(x, axis):
    n = lax.axis_size(axis)
    k = 1
    while k < n:
        x = x + lax.ppermute(x, axis, [(i, i ^ k) for i in range(n)])
        k *= 2
    return x


def shards(
    activations, out_grad, basis, first_moment, second_moment, gain_partial, gain_first, gain_second
):
    tensors = lax.axis_size("tensor")
    shard_count = lax.axis_size("shard")
    shard_pos = lax.axis_index("shard")
    tensor_pos = lax.axis_index("tensor")
    layer_count = activations.shape[0]
    rows_here = basis.shape[1]
    rank_rows = first_moment.shape[1]
    cols_here = out_grad.shape[2]
    rank = basis.shape[2]
    out_rows = rows_here // tensors
    layer_index = 0
    tokens_in = activations[layer_index]
    grads_out = out_grad[layer_index]
    basis_here = basis[layer_index]

    partial_grad = lax.dot_general(
        tokens_in, grads_out, (((0,), (0,)), ((), ())), preferred_element_type=jnp.float32
    )
    grad_block = lax.psum_scatter(partial_grad, "shard", scatter_dimension=0, tiled=True)
    part_proj = jnp.dot(basis_here.T, grad_block, precision=exact_mode)
    gain_row = gain_partial[layer_index, 0]
    gain_len = gain_row.shape[0]
    gain_rows = -(-gain_len // cols_here)
    gain_block = jnp.pad(gain_row, (0, gain_rows * cols_here - gain_len)).reshape(gain_rows, cols_here)
    extra = jnp.zeros((PAD - gain_rows % PAD, cols_here), jnp.float32)
    packed = lax.psum(jnp.concatenate([part_proj, gain_block, extra], axis=0), "shard")
    proj_full = packed[:rank]
    gain_total = packed[rank:rank + gain_rows].reshape(-1)[:gain_len]
    proj_rows = lax.dynamic_slice_in_dim(proj_full, shard_pos * rank_rows, rank_rows, 0)

    square_part = jnp.sum(grad_block * grad_block)
    refresh_part = lax.dot_general(
        grad_block, proj_full, (((1,), (1,)), ((), ())), precision=exact_mode
    )
    extra_r = jnp.zeros((PAD, rank), jnp.float32).at[0, 0].set(square_part)
    packed_r = butterfly_sum(jnp.concatenate([refresh_part, extra_r], axis=0), "tensor")
    gathered = lax.all_gather(packed_r, "shard", axis=0, tiled=False)
    refreshed = gathered[:, :rows_here].reshape(shard_count * rows_here, rank)
    square_st = jnp.sum(gathered[:, rows_here, 0])

    gain_own = lax.dynamic_slice_in_dim(gain_total, shard_pos * rows_here, rows_here, 0)
    square_local = square_st + jnp.sum(gain_total * gain_total)
    total_sq = lax.psum(square_local, "section")
    entry_count = float(lax.axis_size("section") * layer_count * (D * FF + D))
    clip = jnp.minimum(1.0, lax.rsqrt(total_sq / entry_count + clip_eps))

    first_new, second_new, direction = adam_direction(
        clip * proj_rows, first_moment[layer_index], second_moment[layer_index]
    )
    update_here = jnp.dot(
        basis_here, lax.all_gather(direction, "shard", axis=0, tiled=True), precision=exact_mode
    )

    current = refreshed / jnp.sqrt(jnp.sum(refreshed * refreshed) + ns_eps)
    for step_index in range(NS_STEPS - 1):
        current = coef_first * current + jnp.dot(current, mixer_of(current), precision=exact_mode)
    row_start = shard_pos * rows_here + tensor_pos * out_rows
    own = lax.dynamic_slice_in_dim(current, row_start, out_rows, 0)
    own = coef_first * own + jnp.dot(own, mixer_of(current), precision=exact_mode)

    gain_first_new, gain_second_new, gain_dir = adam_direction(
        clip * gain_own, gain_first[layer_index], gain_second[layer_index]
    )
    return (
        update_here[None],
        first_new[None],
        second_new[None],
        own[None],
        gain_dir[None],
        gain_first_new[None],
        gain_second_new[None],
    )


def solution(mesh):
    placed = (
        P("section", "shard", None),
        P("section", "shard", "tensor"),
        P("section", "shard", None),
        P("section", "shard", "tensor"),
        P("section", "shard", "tensor"),
        P("section", "shard", None),
        P("section", "shard"),
        P("section", "shard"),
    )
    return jax.shard_map(
        shards,
        mesh=mesh,
        in_specs=placed,
        out_specs=(
            P("section", "shard", "tensor"),
            P("section", "shard", "tensor"),
            P("section", "shard", "tensor"),
            P("section", ("shard", "tensor"), None),
            P("section", "shard"),
            P("section", "shard"),
            P("section", "shard"),
        ),
        check_vma=False,
    )
```

```python
import jax
import jax.numpy as jnp
from jax import lax
from jax.sharding import PartitionSpec as P

D = 2048
FF = 8192
NS_STEPS = 5
STEP = 8


exact_mode = lax.Precision.HIGHEST
beta_one = 0.9
beta_two = 0.999
adam_eps = 1e-08
clip_eps = 1e-06
ns_eps = 1e-07
coef_first = 3.4445
coef_second = -4.775
coef_third = 2.0315
PAD = 8
SHARD = ("chip_y", "core")


def adam_direction(clipped, first_old, second_old):
    first_new = beta_one * first_old + (1.0 - beta_one) * clipped
    second_new = beta_two * second_old + (1.0 - beta_two) * clipped * clipped
    direction = (
        first_new
        / (1.0 - beta_one**STEP)
        / (jnp.sqrt(second_new / (1.0 - beta_two**STEP)) + adam_eps)
    )
    return (first_new, second_new, direction)


def mixer_of(current):
    gram = jnp.dot(current.T, current, precision=exact_mode)
    return coef_second * gram + coef_third * jnp.dot(gram, gram, precision=exact_mode)


def split3(x):
    hi = lax.reduce_precision(x, exponent_bits=8, mantissa_bits=7)
    rest = x - hi
    mid = lax.reduce_precision(rest, exponent_bits=8, mantissa_bits=7)
    lo = rest - mid
    return tuple(p.astype(jnp.bfloat16) for p in (hi, mid, lo))


def dot_split(lhs, rhs_pieces, dims):
    out = None
    for piece in rhs_pieces:
        term = lax.dot_general(lhs, piece, dims, preferred_element_type=jnp.float32)
        out = term if out is None else out + term
    return out


def butterfly_sum(x, axis):
    n = lax.axis_size(axis)
    k = 1
    while k < n:
        x = x + lax.ppermute(x, axis, [(i, i ^ k) for i in range(n)])
        k *= 2
    return x


def chip_then_y_sum(x):
    core = lax.axis_index("core")
    half = x.shape[0] // 2
    swap = [(0, 1), (1, 0)]
    mine = lax.dynamic_slice_in_dim(x, core * half, half, 0)
    theirs = lax.dynamic_slice_in_dim(x, (1 - core) * half, half, 0)
    mine = mine + lax.ppermute(theirs, "core", swap)
    mine = lax.psum(mine, "chip_y")
    other = lax.ppermute(mine, "core", swap)
    first = jnp.where(core == 0, mine, other)
    second = jnp.where(core == 0, other, mine)
    return jnp.concatenate([first, second], axis=0)


def shards(
    activations, out_grad, basis, first_moment, second_moment, gain_partial, gain_first, gain_second
):
    tensors = lax.axis_size("tensor")
    shard_count = lax.axis_size(SHARD)
    shard_pos = lax.axis_index(SHARD)
    tensor_pos = lax.axis_index("tensor")
    layer_count = activations.shape[0]
    rows_here = basis.shape[1]
    rank_rows = first_moment.shape[1]
    cols_here = out_grad.shape[2]
    rank = basis.shape[2]
    out_rows = rows_here // tensors
    layer_index = 0
    tokens_in = activations[layer_index]
    grads_out = out_grad[layer_index]
    basis_here = basis[layer_index]

    partial_grad = lax.dot_general(
        tokens_in, grads_out, (((0,), (0,)), ((), ())), preferred_element_type=jnp.float32
    )
    grad_block = lax.psum_scatter(partial_grad, SHARD, scatter_dimension=0, tiled=True)
    part_proj = jnp.dot(basis_here.T, grad_block, precision=exact_mode)
    gain_row = gain_partial[layer_index, 0]
    gain_len = gain_row.shape[0]
    gain_rows = -(-gain_len // cols_here)
    gain_block = jnp.pad(gain_row, (0, gain_rows * cols_here - gain_len)).reshape(gain_rows, cols_here)
    extra = jnp.zeros((2 * PAD - gain_rows % (2 * PAD), cols_here), jnp.float32)
    packed = chip_then_y_sum(jnp.concatenate([part_proj, gain_block, extra], axis=0))
    proj_full = packed[:rank]
    gain_total = packed[rank:rank + gain_rows].reshape(-1)[:gain_len]
    proj_rows = lax.dynamic_slice_in_dim(proj_full, shard_pos * rank_rows, rank_rows, 0)

    square_part = jnp.sum(grad_block * grad_block)
    refresh_part = lax.dot_general(
        grad_block, proj_full, (((1,), (1,)), ((), ())), precision=exact_mode
    )
    extra_r = jnp.zeros((PAD, rank), jnp.float32).at[0, 0].set(square_part)
    packed_r = butterfly_sum(jnp.concatenate([refresh_part, extra_r], axis=0), "tensor")
    gathered = lax.all_gather(packed_r, SHARD, axis=0, tiled=False)
    refreshed = gathered[:, :rows_here].reshape(shard_count * rows_here, rank)
    square_st = jnp.sum(gathered[:, rows_here, 0])

    gain_own = lax.dynamic_slice_in_dim(gain_total, shard_pos * rows_here, rows_here, 0)
    square_local = square_st + jnp.sum(gain_total * gain_total)
    total_sq = butterfly_sum(jnp.full((PAD, 128), square_local, jnp.float32), "section")[0, 0]
    entry_count = float(lax.axis_size("section") * layer_count * (D * FF + D))
    clip = jnp.minimum(1.0, lax.rsqrt(total_sq / entry_count + clip_eps))

    first_new, second_new, direction = adam_direction(
        clip * proj_rows, first_moment[layer_index], second_moment[layer_index]
    )
    update_here = jnp.dot(
        basis_here, lax.all_gather(direction, SHARD, axis=0, tiled=True), precision=exact_mode
    )

    current = refreshed / jnp.sqrt(jnp.sum(refreshed * refreshed) + ns_eps)
    for step_index in range(NS_STEPS - 1):
        current = coef_first * current + jnp.dot(current, mixer_of(current), precision=exact_mode)
    row_start = shard_pos * rows_here + tensor_pos * out_rows
    own = lax.dynamic_slice_in_dim(current, row_start, out_rows, 0)
    own = coef_first * own + jnp.dot(own, mixer_of(current), precision=exact_mode)

    gain_first_new, gain_second_new, gain_dir = adam_direction(
        clip * gain_own, gain_first[layer_index], gain_second[layer_index]
    )
    return (
        update_here[None],
        first_new[None],
        second_new[None],
        own[None],
        gain_dir[None],
        gain_first_new[None],
        gain_second_new[None],
    )


def solution(mesh):
    names = mesh.axis_names
    sizes = dict(mesh.shape)
    chip_y = sizes["shard"] // 2
    split_shape = []
    split_names = []
    for name in names:
        if name == "shard":
            split_shape += [chip_y, 2]
            split_names += ["chip_y", "core"]
        else:
            split_shape.append(sizes[name])
            split_names.append(name)
    split = jax.sharding.Mesh(mesh.devices.reshape(split_shape), tuple(split_names))
    placed = (
        P("section", SHARD, None),
        P("section", SHARD, "tensor"),
        P("section", SHARD, None),
        P("section", SHARD, "tensor"),
        P("section", SHARD, "tensor"),
        P("section", SHARD, None),
        P("section", SHARD),
        P("section", SHARD),
    )
    return jax.shard_map(
        shards,
        mesh=split,
        in_specs=placed,
        out_specs=(
            P("section", SHARD, "tensor"),
            P("section", SHARD, "tensor"),
            P("section", SHARD, "tensor"),
            P("section", SHARD + ("tensor",), None),
            P("section", SHARD),
            P("section", SHARD),
            P("section", SHARD),
        ),
        check_vma=False,
    )
```

```python
import jax
import jax.numpy as jnp
from jax import lax
from jax.sharding import PartitionSpec as P

D = 2048
FF = 8192
NS_STEPS = 5
STEP = 8


exact_mode = lax.Precision.HIGHEST
beta_one = 0.9
beta_two = 0.999
adam_eps = 1e-08
clip_eps = 1e-06
ns_eps = 1e-07
coef_first = 3.4445
coef_second = -4.775
coef_third = 2.0315
PAD = 8
SHARD = ("chip_y", "core")


def adam_direction(clipped, first_old, second_old):
    first_new = beta_one * first_old + (1.0 - beta_one) * clipped
    second_new = beta_two * second_old + (1.0 - beta_two) * clipped * clipped
    direction = (
        first_new
        / (1.0 - beta_one**STEP)
        / (jnp.sqrt(second_new / (1.0 - beta_two**STEP)) + adam_eps)
    )
    return (first_new, second_new, direction)


def mixer_of(current):
    gram = jnp.dot(current.T, current, precision=exact_mode)
    return coef_second * gram + coef_third * jnp.dot(gram, gram, precision=exact_mode)


def split3(x):
    hi = lax.reduce_precision(x, exponent_bits=8, mantissa_bits=7)
    rest = x - hi
    mid = lax.reduce_precision(rest, exponent_bits=8, mantissa_bits=7)
    lo = rest - mid
    return tuple(p.astype(jnp.bfloat16) for p in (hi, mid, lo))


def dot_split(lhs, rhs_pieces, dims):
    out = None
    for piece in rhs_pieces:
        term = lax.dot_general(lhs, piece, dims, preferred_element_type=jnp.float32)
        out = term if out is None else out + term
    return out


def butterfly_sum(x, axis):
    n = lax.axis_size(axis)
    k = 1
    while k < n:
        x = x + lax.ppermute(x, axis, [(i, i ^ k) for i in range(n)])
        k *= 2
    return x


def chip_then_y_sum(x):
    core = lax.axis_index("core")
    half = x.shape[0] // 2
    swap = [(0, 1), (1, 0)]
    mine = lax.dynamic_slice_in_dim(x, core * half, half, 0)
    theirs = lax.dynamic_slice_in_dim(x, (1 - core) * half, half, 0)
    mine = mine + lax.ppermute(theirs, "core", swap)
    mine = lax.psum(mine, "chip_y")
    other = lax.ppermute(mine, "core", swap)
    first = jnp.where(core == 0, mine, other)
    second = jnp.where(core == 0, other, mine)
    return jnp.concatenate([first, second], axis=0)


def shards(
    activations, out_grad, basis, first_moment, second_moment, gain_partial, gain_first, gain_second
):
    tensors = lax.axis_size("tensor")
    shard_count = lax.axis_size(SHARD)
    shard_pos = lax.axis_index(SHARD)
    tensor_pos = lax.axis_index("tensor")
    layer_count = activations.shape[0]
    rows_here = basis.shape[1]
    rank_rows = first_moment.shape[1]
    cols_here = out_grad.shape[2]
    rank = basis.shape[2]
    out_rows = rows_here // tensors
    layer_index = 0
    tokens_in = activations[layer_index]
    grads_out = out_grad[layer_index]
    basis_here = basis[layer_index]

    partial_grad = lax.dot_general(
        tokens_in, grads_out, (((0,), (0,)), ((), ())), preferred_element_type=jnp.float32
    )
    grad_block = lax.psum_scatter(partial_grad, SHARD, scatter_dimension=0, tiled=True)
    part_proj = jnp.dot(basis_here.T, grad_block, precision=exact_mode)
    gain_row = gain_partial[layer_index, 0]
    gain_len = gain_row.shape[0]
    gain_rows = -(-gain_len // cols_here)
    gain_block = jnp.pad(gain_row, (0, gain_rows * cols_here - gain_len)).reshape(gain_rows, cols_here)
    square_part = jnp.sum(grad_block * grad_block)
    extra = jnp.zeros((2 * PAD - gain_rows % (2 * PAD), cols_here), jnp.float32).at[0, 0].set(square_part)
    packed = chip_then_y_sum(jnp.concatenate([part_proj, gain_block, extra], axis=0))
    proj_full = packed[:rank]
    square_shard = packed[rank + gain_rows, 0]
    gain_total = packed[rank:rank + gain_rows].reshape(-1)[:gain_len]
    proj_rows = lax.dynamic_slice_in_dim(proj_full, shard_pos * rank_rows, rank_rows, 0)

    refresh_part = lax.dot_general(
        grad_block, proj_full, (((1,), (1,)), ((), ())), precision=exact_mode
    )
    extra_r = jnp.zeros((PAD, rank), jnp.float32).at[0, 0].set(square_shard)
    packed_r = butterfly_sum(jnp.concatenate([refresh_part, extra_r], axis=0), "tensor")
    square_st = packed_r[rows_here, 0]
    refreshed = lax.all_gather(packed_r[:rows_here], SHARD, axis=0, tiled=True)

    gain_own = lax.dynamic_slice_in_dim(gain_total, shard_pos * rows_here, rows_here, 0)
    square_local = square_st + jnp.sum(gain_total * gain_total)
    total_sq = butterfly_sum(jnp.full((PAD, 128), square_local, jnp.float32), "section")[0, 0]
    entry_count = float(lax.axis_size("section") * layer_count * (D * FF + D))
    clip = jnp.minimum(1.0, lax.rsqrt(total_sq / entry_count + clip_eps))

    first_new, second_new, direction = adam_direction(
        clip * proj_rows, first_moment[layer_index], second_moment[layer_index]
    )
    update_here = jnp.dot(
        basis_here, lax.all_gather(direction, SHARD, axis=0, tiled=True), precision=exact_mode
    )

    current = refreshed / jnp.sqrt(jnp.sum(refreshed * refreshed) + ns_eps)
    for step_index in range(NS_STEPS - 1):
        current = coef_first * current + jnp.dot(current, mixer_of(current), precision=exact_mode)
    row_start = shard_pos * rows_here + tensor_pos * out_rows
    own = lax.dynamic_slice_in_dim(current, row_start, out_rows, 0)
    own = coef_first * own + jnp.dot(own, mixer_of(current), precision=exact_mode)

    gain_first_new, gain_second_new, gain_dir = adam_direction(
        clip * gain_own, gain_first[layer_index], gain_second[layer_index]
    )
    return (
        update_here[None],
        first_new[None],
        second_new[None],
        own[None],
        gain_dir[None],
        gain_first_new[None],
        gain_second_new[None],
    )


def solution(mesh):
    names = mesh.axis_names
    sizes = dict(mesh.shape)
    chip_y = sizes["shard"] // 2
    split_shape = []
    split_names = []
    for name in names:
        if name == "shard":
            split_shape += [chip_y, 2]
            split_names += ["chip_y", "core"]
        else:
            split_shape.append(sizes[name])
            split_names.append(name)
    split = jax.sharding.Mesh(mesh.devices.reshape(split_shape), tuple(split_names))
    placed = (
        P("section", SHARD, None),
        P("section", SHARD, "tensor"),
        P("section", SHARD, None),
        P("section", SHARD, "tensor"),
        P("section", SHARD, "tensor"),
        P("section", SHARD, None),
        P("section", SHARD),
        P("section", SHARD),
    )
    return jax.shard_map(
        shards,
        mesh=split,
        in_specs=placed,
        out_specs=(
            P("section", SHARD, "tensor"),
            P("section", SHARD, "tensor"),
            P("section", SHARD, "tensor"),
            P("section", SHARD + ("tensor",), None),
            P("section", SHARD),
            P("section", SHARD),
            P("section", SHARD),
        ),
        check_vma=False,
    )
```

```python
import jax
import jax.numpy as jnp
from jax import lax
from jax.sharding import PartitionSpec as P

D = 2048
FF = 8192
NS_STEPS = 5
STEP = 8


exact_mode = lax.Precision.HIGHEST
beta_one = 0.9
beta_two = 0.999
adam_eps = 1e-08
clip_eps = 1e-06
ns_eps = 1e-07
coef_first = 3.4445
coef_second = -4.775
coef_third = 2.0315
PAD = 8
SHARD = ("chip_y", "core")


def adam_direction(clipped, first_old, second_old):
    first_new = beta_one * first_old + (1.0 - beta_one) * clipped
    second_new = beta_two * second_old + (1.0 - beta_two) * clipped * clipped
    direction = (
        first_new
        / (1.0 - beta_one**STEP)
        / (jnp.sqrt(second_new / (1.0 - beta_two**STEP)) + adam_eps)
    )
    return (first_new, second_new, direction)


ns_mode = lax.Precision.HIGH


def mixer_of(current):
    gram = jnp.dot(current.T, current, precision=ns_mode)
    return coef_second * gram + coef_third * jnp.dot(gram, gram, precision=ns_mode)


def split3(x):
    hi = lax.reduce_precision(x, exponent_bits=8, mantissa_bits=7)
    rest = x - hi
    mid = lax.reduce_precision(rest, exponent_bits=8, mantissa_bits=7)
    lo = rest - mid
    return tuple(p.astype(jnp.bfloat16) for p in (hi, mid, lo))


def dot_split(lhs, rhs_pieces, dims):
    out = None
    for piece in rhs_pieces:
        term = lax.dot_general(lhs, piece, dims, preferred_element_type=jnp.float32)
        out = term if out is None else out + term
    return out


def butterfly_sum(x, axis):
    n = lax.axis_size(axis)
    k = 1
    while k < n:
        x = x + lax.ppermute(x, axis, [(i, i ^ k) for i in range(n)])
        k *= 2
    return x


def chip_then_y_sum(x):
    core = lax.axis_index("core")
    half = x.shape[0] // 2
    swap = [(0, 1), (1, 0)]
    mine = lax.dynamic_slice_in_dim(x, core * half, half, 0)
    theirs = lax.dynamic_slice_in_dim(x, (1 - core) * half, half, 0)
    mine = mine + lax.ppermute(theirs, "core", swap)
    mine = lax.psum(mine, "chip_y")
    other = lax.ppermute(mine, "core", swap)
    first = jnp.where(core == 0, mine, other)
    second = jnp.where(core == 0, other, mine)
    return jnp.concatenate([first, second], axis=0)


def shards(
    activations, out_grad, basis, first_moment, second_moment, gain_partial, gain_first, gain_second
):
    tensors = lax.axis_size("tensor")
    shard_count = lax.axis_size(SHARD)
    shard_pos = lax.axis_index(SHARD)
    tensor_pos = lax.axis_index("tensor")
    layer_count = activations.shape[0]
    rows_here = basis.shape[1]
    rank_rows = first_moment.shape[1]
    cols_here = out_grad.shape[2]
    rank = basis.shape[2]
    out_rows = rows_here // tensors
    layer_index = 0
    tokens_in = activations[layer_index]
    grads_out = out_grad[layer_index]
    basis_here = basis[layer_index]

    partial_grad = lax.dot_general(
        tokens_in, grads_out, (((0,), (0,)), ((), ())), preferred_element_type=jnp.float32
    )
    grad_block = lax.psum_scatter(partial_grad, SHARD, scatter_dimension=0, tiled=True)
    part_proj = jnp.dot(basis_here.T, grad_block, precision=exact_mode)
    gain_row = gain_partial[layer_index, 0]
    gain_len = gain_row.shape[0]
    gain_rows = -(-gain_len // cols_here)
    gain_block = jnp.pad(gain_row, (0, gain_rows * cols_here - gain_len)).reshape(gain_rows, cols_here)
    square_part = jnp.sum(grad_block * grad_block)
    extra = jnp.zeros((2 * PAD - gain_rows % (2 * PAD), cols_here), jnp.float32).at[0, 0].set(square_part)
    packed = chip_then_y_sum(jnp.concatenate([part_proj, gain_block, extra], axis=0))
    proj_full = packed[:rank]
    square_shard = packed[rank + gain_rows, 0]
    gain_total = packed[rank:rank + gain_rows].reshape(-1)[:gain_len]
    proj_rows = lax.dynamic_slice_in_dim(proj_full, shard_pos * rank_rows, rank_rows, 0)

    refresh_part = lax.dot_general(
        grad_block, proj_full, (((1,), (1,)), ((), ())), precision=exact_mode
    )
    extra_r = jnp.zeros((PAD, rank), jnp.float32).at[0, 0].set(square_shard)
    packed_r = butterfly_sum(jnp.concatenate([refresh_part, extra_r], axis=0), "tensor")
    square_st = packed_r[rows_here, 0]
    refreshed = lax.all_gather(packed_r[:rows_here], SHARD, axis=0, tiled=True)

    gain_own = lax.dynamic_slice_in_dim(gain_total, shard_pos * rows_here, rows_here, 0)
    square_local = square_st + jnp.sum(gain_total * gain_total)
    total_sq = butterfly_sum(jnp.full((PAD, 128), square_local, jnp.float32), "section")[0, 0]
    entry_count = float(lax.axis_size("section") * layer_count * (D * FF + D))
    clip = jnp.minimum(1.0, lax.rsqrt(total_sq / entry_count + clip_eps))

    first_new, second_new, direction = adam_direction(
        clip * proj_rows, first_moment[layer_index], second_moment[layer_index]
    )
    update_here = jnp.dot(
        basis_here, lax.all_gather(direction, SHARD, axis=0, tiled=True), precision=exact_mode
    )

    current = refreshed / jnp.sqrt(jnp.sum(refreshed * refreshed) + ns_eps)
    for step_index in range(NS_STEPS - 1):
        current = coef_first * current + jnp.dot(current, mixer_of(current), precision=ns_mode)
    row_start = shard_pos * rows_here + tensor_pos * out_rows
    own = lax.dynamic_slice_in_dim(current, row_start, out_rows, 0)
    own = coef_first * own + jnp.dot(own, mixer_of(current), precision=ns_mode)

    gain_first_new, gain_second_new, gain_dir = adam_direction(
        clip * gain_own, gain_first[layer_index], gain_second[layer_index]
    )
    return (
        update_here[None],
        first_new[None],
        second_new[None],
        own[None],
        gain_dir[None],
        gain_first_new[None],
        gain_second_new[None],
    )


def solution(mesh):
    names = mesh.axis_names
    sizes = dict(mesh.shape)
    chip_y = sizes["shard"] // 2
    split_shape = []
    split_names = []
    for name in names:
        if name == "shard":
            split_shape += [chip_y, 2]
            split_names += ["chip_y", "core"]
        else:
            split_shape.append(sizes[name])
            split_names.append(name)
    split = jax.sharding.Mesh(mesh.devices.reshape(split_shape), tuple(split_names))
    placed = (
        P("section", SHARD, None),
        P("section", SHARD, "tensor"),
        P("section", SHARD, None),
        P("section", SHARD, "tensor"),
        P("section", SHARD, "tensor"),
        P("section", SHARD, None),
        P("section", SHARD),
        P("section", SHARD),
    )
    return jax.shard_map(
        shards,
        mesh=split,
        in_specs=placed,
        out_specs=(
            P("section", SHARD, "tensor"),
            P("section", SHARD, "tensor"),
            P("section", SHARD, "tensor"),
            P("section", SHARD + ("tensor",), None),
            P("section", SHARD),
            P("section", SHARD),
            P("section", SHARD),
        ),
        check_vma=False,
    )
```

```python
import jax
import jax.numpy as jnp
from jax import lax
from jax.sharding import PartitionSpec as P

D = 2048
FF = 8192
NS_STEPS = 5
STEP = 8


exact_mode = lax.Precision.HIGHEST
beta_one = 0.9
beta_two = 0.999
adam_eps = 1e-08
clip_eps = 1e-06
ns_eps = 1e-07
coef_first = 3.4445
coef_second = -4.775
coef_third = 2.0315
PAD = 8
SHARD = ("chip_y", "core")


def adam_direction(clipped, first_old, second_old):
    first_new = beta_one * first_old + (1.0 - beta_one) * clipped
    second_new = beta_two * second_old + (1.0 - beta_two) * clipped * clipped
    direction = (
        first_new
        / (1.0 - beta_one**STEP)
        / (jnp.sqrt(second_new / (1.0 - beta_two**STEP)) + adam_eps)
    )
    return (first_new, second_new, direction)


ns_mode = lax.Precision.HIGH


def mixer_of(current):
    gram = jnp.dot(current.T, current, precision=ns_mode)
    return coef_second * gram + coef_third * jnp.dot(gram, gram, precision=ns_mode)


def split3(x):
    hi = lax.reduce_precision(x, exponent_bits=8, mantissa_bits=7)
    rest = x - hi
    mid = lax.reduce_precision(rest, exponent_bits=8, mantissa_bits=7)
    lo = rest - mid
    return tuple(p.astype(jnp.bfloat16) for p in (hi, mid, lo))


def dot_split(lhs, rhs_pieces, dims):
    out = None
    for piece in rhs_pieces:
        term = lax.dot_general(lhs, piece, dims, preferred_element_type=jnp.float32)
        out = term if out is None else out + term
    return out


def butterfly_sum(x, axis):
    n = lax.axis_size(axis)
    k = 1
    while k < n:
        x = x + lax.ppermute(x, axis, [(i, i ^ k) for i in range(n)])
        k *= 2
    return x


def chip_then_y_sum(x):
    core = lax.axis_index("core")
    half = x.shape[0] // 2
    swap = [(0, 1), (1, 0)]
    mine = lax.dynamic_slice_in_dim(x, core * half, half, 0)
    theirs = lax.dynamic_slice_in_dim(x, (1 - core) * half, half, 0)
    mine = mine + lax.ppermute(theirs, "core", swap)
    mine = lax.psum(mine, "chip_y")
    other = lax.ppermute(mine, "core", swap)
    first = jnp.where(core == 0, mine, other)
    second = jnp.where(core == 0, other, mine)
    return jnp.concatenate([first, second], axis=0)


def gather_doubling(x):
    n = lax.axis_size(SHARD)
    pos = lax.axis_index(SHARD)
    buf = x
    k = 1
    while k < n:
        other = lax.ppermute(buf, SHARD, [(i, i ^ k) for i in range(n)])
        low = (pos // k) % 2 == 0
        buf = jnp.where(low, jnp.concatenate([buf, other], 0), jnp.concatenate([other, buf], 0))
        k *= 2
    return buf


def shards(
    activations, out_grad, basis, first_moment, second_moment, gain_partial, gain_first, gain_second
):
    tensors = lax.axis_size("tensor")
    shard_count = lax.axis_size(SHARD)
    shard_pos = lax.axis_index(SHARD)
    tensor_pos = lax.axis_index("tensor")
    layer_count = activations.shape[0]
    rows_here = basis.shape[1]
    rank_rows = first_moment.shape[1]
    cols_here = out_grad.shape[2]
    rank = basis.shape[2]
    out_rows = rows_here // tensors
    layer_index = 0
    tokens_in = activations[layer_index]
    grads_out = out_grad[layer_index]
    basis_here = basis[layer_index]

    partial_grad = lax.dot_general(
        tokens_in, grads_out, (((0,), (0,)), ((), ())), preferred_element_type=jnp.float32
    )
    grad_block = lax.psum_scatter(partial_grad, SHARD, scatter_dimension=0, tiled=True)
    part_proj = jnp.dot(basis_here.T, grad_block, precision=exact_mode)
    gain_row = gain_partial[layer_index, 0]
    gain_len = gain_row.shape[0]
    gain_rows = -(-gain_len // cols_here)
    gain_block = jnp.pad(gain_row, (0, gain_rows * cols_here - gain_len)).reshape(gain_rows, cols_here)
    square_part = jnp.sum(grad_block * grad_block)
    extra = jnp.zeros((2 * PAD - gain_rows % (2 * PAD), cols_here), jnp.float32).at[0, 0].set(square_part)
    packed = chip_then_y_sum(jnp.concatenate([part_proj, gain_block, extra], axis=0))
    proj_full = packed[:rank]
    square_shard = packed[rank + gain_rows, 0]
    gain_total = packed[rank:rank + gain_rows].reshape(-1)[:gain_len]
    proj_rows = lax.dynamic_slice_in_dim(proj_full, shard_pos * rank_rows, rank_rows, 0)

    refresh_part = lax.dot_general(
        grad_block, proj_full, (((1,), (1,)), ((), ())), precision=exact_mode
    )
    extra_r = jnp.zeros((PAD, rank), jnp.float32).at[0, 0].set(square_shard)
    packed_r = butterfly_sum(jnp.concatenate([refresh_part, extra_r], axis=0), "tensor")
    square_st = packed_r[rows_here, 0]
    refreshed = lax.all_gather(packed_r[:rows_here], SHARD, axis=0, tiled=True)

    gain_own = lax.dynamic_slice_in_dim(gain_total, shard_pos * rows_here, rows_here, 0)
    square_local = square_st + jnp.sum(gain_total * gain_total)
    total_sq = butterfly_sum(jnp.full((PAD, 128), square_local, jnp.float32), "section")[0, 0]
    entry_count = float(lax.axis_size("section") * layer_count * (D * FF + D))
    clip = jnp.minimum(1.0, lax.rsqrt(total_sq / entry_count + clip_eps))

    first_new, second_new, direction = adam_direction(
        clip * proj_rows, first_moment[layer_index], second_moment[layer_index]
    )
    update_here = jnp.dot(
        basis_here, gather_doubling(direction), precision=exact_mode
    )

    current = refreshed / jnp.sqrt(jnp.sum(refreshed * refreshed) + ns_eps)
    for step_index in range(NS_STEPS - 1):
        current = coef_first * current + jnp.dot(current, mixer_of(current), precision=ns_mode)
    row_start = shard_pos * rows_here + tensor_pos * out_rows
    own = lax.dynamic_slice_in_dim(current, row_start, out_rows, 0)
    own = coef_first * own + jnp.dot(own, mixer_of(current), precision=ns_mode)

    gain_first_new, gain_second_new, gain_dir = adam_direction(
        clip * gain_own, gain_first[layer_index], gain_second[layer_index]
    )
    return (
        update_here[None],
        first_new[None],
        second_new[None],
        own[None],
        gain_dir[None],
        gain_first_new[None],
        gain_second_new[None],
    )


def solution(mesh):
    names = mesh.axis_names
    sizes = dict(mesh.shape)
    chip_y = sizes["shard"] // 2
    split_shape = []
    split_names = []
    for name in names:
        if name == "shard":
            split_shape += [chip_y, 2]
            split_names += ["chip_y", "core"]
        else:
            split_shape.append(sizes[name])
            split_names.append(name)
    split = jax.sharding.Mesh(mesh.devices.reshape(split_shape), tuple(split_names))
    placed = (
        P("section", SHARD, None),
        P("section", SHARD, "tensor"),
        P("section", SHARD, None),
        P("section", SHARD, "tensor"),
        P("section", SHARD, "tensor"),
        P("section", SHARD, None),
        P("section", SHARD),
        P("section", SHARD),
    )
    return jax.shard_map(
        shards,
        mesh=split,
        in_specs=placed,
        out_specs=(
            P("section", SHARD, "tensor"),
            P("section", SHARD, "tensor"),
            P("section", SHARD, "tensor"),
            P("section", SHARD + ("tensor",), None),
            P("section", SHARD),
            P("section", SHARD),
            P("section", SHARD),
        ),
        check_vma=False,
    )
```

```python
import jax
import jax.numpy as jnp
from jax import lax
from jax.sharding import PartitionSpec as P

D = 2048
FF = 8192
NS_STEPS = 5
STEP = 8


exact_mode = lax.Precision.HIGHEST
beta_one = 0.9
beta_two = 0.999
adam_eps = 1e-08
clip_eps = 1e-06
ns_eps = 1e-07
coef_first = 3.4445
coef_second = -4.775
coef_third = 2.0315
PAD = 8
SHARD = ("chip_y", "core")


def adam_direction(clipped, first_old, second_old):
    first_new = beta_one * first_old + (1.0 - beta_one) * clipped
    second_new = beta_two * second_old + (1.0 - beta_two) * clipped * clipped
    direction = (
        first_new
        / (1.0 - beta_one**STEP)
        / (jnp.sqrt(second_new / (1.0 - beta_two**STEP)) + adam_eps)
    )
    return (first_new, second_new, direction)


ns_mode = lax.Precision.HIGH


def mixer_of(current):
    gram = jnp.dot(current.T, current, precision=ns_mode)
    return coef_second * gram + coef_third * jnp.dot(gram, gram, precision=ns_mode)


def split3(x):
    hi = lax.reduce_precision(x, exponent_bits=8, mantissa_bits=7)
    rest = x - hi
    mid = lax.reduce_precision(rest, exponent_bits=8, mantissa_bits=7)
    lo = rest - mid
    return tuple(p.astype(jnp.bfloat16) for p in (hi, mid, lo))


def dot_split(lhs, rhs_pieces, dims):
    out = None
    for piece in rhs_pieces:
        term = lax.dot_general(lhs, piece, dims, preferred_element_type=jnp.float32)
        out = term if out is None else out + term
    return out


def butterfly_sum(x, axis):
    n = lax.axis_size(axis)
    k = 1
    while k < n:
        x = x + lax.ppermute(x, axis, [(i, i ^ k) for i in range(n)])
        k *= 2
    return x


def chip_then_y_sum(x):
    core = lax.axis_index("core")
    half = x.shape[0] // 2
    swap = [(0, 1), (1, 0)]
    mine = lax.dynamic_slice_in_dim(x, core * half, half, 0)
    theirs = lax.dynamic_slice_in_dim(x, (1 - core) * half, half, 0)
    mine = mine + lax.ppermute(theirs, "core", swap)
    mine = lax.psum(mine, "chip_y")
    other = lax.ppermute(mine, "core", swap)
    first = jnp.where(core == 0, mine, other)
    second = jnp.where(core == 0, other, mine)
    return jnp.concatenate([first, second], axis=0)


def shards(
    activations, out_grad, basis, first_moment, second_moment, gain_partial, gain_first, gain_second
):
    tensors = lax.axis_size("tensor")
    shard_count = lax.axis_size(SHARD)
    shard_pos = lax.axis_index(SHARD)
    tensor_pos = lax.axis_index("tensor")
    layer_count = activations.shape[0]
    rows_here = basis.shape[1]
    rank_rows = first_moment.shape[1]
    cols_here = out_grad.shape[2]
    rank = basis.shape[2]
    out_rows = rows_here // tensors
    layer_index = 0
    tokens_in = activations[layer_index]
    grads_out = out_grad[layer_index]
    basis_here = basis[layer_index]

    col_half = cols_here // 2
    grad_halves = []
    for piece in (grads_out[:, :col_half], grads_out[:, col_half:]):
        partial_grad = lax.dot_general(
            tokens_in, piece, (((0,), (0,)), ((), ())), preferred_element_type=jnp.float32
        )
        grad_halves.append(lax.psum_scatter(partial_grad, SHARD, scatter_dimension=0, tiled=True))
    grad_block = jnp.concatenate(grad_halves, axis=1)
    part_proj = jnp.dot(basis_here.T, grad_block, precision=exact_mode)
    gain_row = gain_partial[layer_index, 0]
    gain_len = gain_row.shape[0]
    gain_rows = -(-gain_len // cols_here)
    gain_block = jnp.pad(gain_row, (0, gain_rows * cols_here - gain_len)).reshape(gain_rows, cols_here)
    square_part = jnp.sum(grad_block * grad_block)
    extra = jnp.zeros((2 * PAD - gain_rows % (2 * PAD), cols_here), jnp.float32).at[0, 0].set(square_part)
    packed = chip_then_y_sum(jnp.concatenate([part_proj, gain_block, extra], axis=0))
    proj_full = packed[:rank]
    square_shard = packed[rank + gain_rows, 0]
    gain_total = packed[rank:rank + gain_rows].reshape(-1)[:gain_len]
    proj_rows = lax.dynamic_slice_in_dim(proj_full, shard_pos * rank_rows, rank_rows, 0)

    refresh_part = lax.dot_general(
        grad_block, proj_full, (((1,), (1,)), ((), ())), precision=exact_mode
    )
    extra_r = jnp.zeros((PAD, rank), jnp.float32).at[0, 0].set(square_shard)
    packed_r = butterfly_sum(jnp.concatenate([refresh_part, extra_r], axis=0), "tensor")
    square_st = packed_r[rows_here, 0]
    refreshed = lax.all_gather(packed_r[:rows_here], SHARD, axis=0, tiled=True)

    gain_own = lax.dynamic_slice_in_dim(gain_total, shard_pos * rows_here, rows_here, 0)
    square_local = square_st + jnp.sum(gain_total * gain_total)
    total_sq = butterfly_sum(jnp.full((PAD, 128), square_local, jnp.float32), "section")[0, 0]
    entry_count = float(lax.axis_size("section") * layer_count * (D * FF + D))
    clip = jnp.minimum(1.0, lax.rsqrt(total_sq / entry_count + clip_eps))

    first_new, second_new, direction = adam_direction(
        clip * proj_rows, first_moment[layer_index], second_moment[layer_index]
    )
    update_here = jnp.dot(
        basis_here, lax.all_gather(direction, SHARD, axis=0, tiled=True), precision=exact_mode
    )

    current = refreshed / jnp.sqrt(jnp.sum(refreshed * refreshed) + ns_eps)
    for step_index in range(NS_STEPS - 1):
        current = coef_first * current + jnp.dot(current, mixer_of(current), precision=ns_mode)
    row_start = shard_pos * rows_here + tensor_pos * out_rows
    own = lax.dynamic_slice_in_dim(current, row_start, out_rows, 0)
    own = coef_first * own + jnp.dot(own, mixer_of(current), precision=ns_mode)

    gain_first_new, gain_second_new, gain_dir = adam_direction(
        clip * gain_own, gain_first[layer_index], gain_second[layer_index]
    )
    return (
        update_here[None],
        first_new[None],
        second_new[None],
        own[None],
        gain_dir[None],
        gain_first_new[None],
        gain_second_new[None],
    )


def solution(mesh):
    names = mesh.axis_names
    sizes = dict(mesh.shape)
    chip_y = sizes["shard"] // 2
    split_shape = []
    split_names = []
    for name in names:
        if name == "shard":
            split_shape += [chip_y, 2]
            split_names += ["chip_y", "core"]
        else:
            split_shape.append(sizes[name])
            split_names.append(name)
    split = jax.sharding.Mesh(mesh.devices.reshape(split_shape), tuple(split_names))
    placed = (
        P("section", SHARD, None),
        P("section", SHARD, "tensor"),
        P("section", SHARD, None),
        P("section", SHARD, "tensor"),
        P("section", SHARD, "tensor"),
        P("section", SHARD, None),
        P("section", SHARD),
        P("section", SHARD),
    )
    return jax.shard_map(
        shards,
        mesh=split,
        in_specs=placed,
        out_specs=(
            P("section", SHARD, "tensor"),
            P("section", SHARD, "tensor"),
            P("section", SHARD, "tensor"),
            P("section", SHARD + ("tensor",), None),
            P("section", SHARD),
            P("section", SHARD),
            P("section", SHARD),
        ),
        check_vma=False,
    )
```

```python
import jax
import jax.numpy as jnp
from jax import lax
from jax.sharding import PartitionSpec as P

D = 2048
FF = 8192
NS_STEPS = 5
STEP = 8


exact_mode = lax.Precision.HIGHEST
beta_one = 0.9
beta_two = 0.999
adam_eps = 1e-08
clip_eps = 1e-06
ns_eps = 1e-07
coef_first = 3.4445
coef_second = -4.775
coef_third = 2.0315
PAD = 8
SHARD = ("chip_y", "core")


def adam_direction(clipped, first_old, second_old):
    first_new = beta_one * first_old + (1.0 - beta_one) * clipped
    second_new = beta_two * second_old + (1.0 - beta_two) * clipped * clipped
    direction = (
        first_new
        / (1.0 - beta_one**STEP)
        / (jnp.sqrt(second_new / (1.0 - beta_two**STEP)) + adam_eps)
    )
    return (first_new, second_new, direction)


ns_mode = lax.Precision.HIGH


def mixer_of(current):
    gram = jnp.dot(current.T, current, precision=ns_mode)
    return coef_second * gram + coef_third * jnp.dot(gram, gram, precision=ns_mode)


def split3(x):
    hi = lax.reduce_precision(x, exponent_bits=8, mantissa_bits=7)
    rest = x - hi
    mid = lax.reduce_precision(rest, exponent_bits=8, mantissa_bits=7)
    lo = rest - mid
    return tuple(p.astype(jnp.bfloat16) for p in (hi, mid, lo))


def dot_split(lhs, rhs_pieces, dims):
    out = None
    for piece in rhs_pieces:
        term = lax.dot_general(lhs, piece, dims, preferred_element_type=jnp.float32)
        out = term if out is None else out + term
    return out


def butterfly_sum(x, axis):
    n = lax.axis_size(axis)
    k = 1
    while k < n:
        x = x + lax.ppermute(x, axis, [(i, i ^ k) for i in range(n)])
        k *= 2
    return x


def chip_then_y_sum(x):
    core = lax.axis_index("core")
    half = x.shape[0] // 2
    swap = [(0, 1), (1, 0)]
    mine = lax.dynamic_slice_in_dim(x, core * half, half, 0)
    theirs = lax.dynamic_slice_in_dim(x, (1 - core) * half, half, 0)
    mine = mine + lax.ppermute(theirs, "core", swap)
    mine = lax.psum(mine, "chip_y")
    other = lax.ppermute(mine, "core", swap)
    first = jnp.where(core == 0, mine, other)
    second = jnp.where(core == 0, other, mine)
    return jnp.concatenate([first, second], axis=0)


def shards(
    activations, out_grad, basis, first_moment, second_moment, gain_partial, gain_first, gain_second
):
    tensors = lax.axis_size("tensor")
    shard_count = lax.axis_size(SHARD)
    shard_pos = lax.axis_index(SHARD)
    tensor_pos = lax.axis_index("tensor")
    layer_count = activations.shape[0]
    rows_here = basis.shape[1]
    rank_rows = first_moment.shape[1]
    cols_here = out_grad.shape[2]
    rank = basis.shape[2]
    out_rows = rows_here // tensors
    layer_index = 0
    tokens_in = activations[layer_index]
    grads_out = out_grad[layer_index]
    basis_here = basis[layer_index]

    partial_grad = lax.dot_general(
        tokens_in, grads_out, (((0,), (0,)), ((), ())), preferred_element_type=jnp.float32
    )
    grad_block = lax.psum_scatter(partial_grad, SHARD, scatter_dimension=0, tiled=True)
    part_proj = jnp.dot(basis_here.T, grad_block, precision=exact_mode)
    gain_row = gain_partial[layer_index, 0]
    gain_len = gain_row.shape[0]
    gain_rows = -(-gain_len // cols_here)
    gain_block = jnp.pad(gain_row, (0, gain_rows * cols_here - gain_len)).reshape(gain_rows, cols_here)
    square_part = jnp.sum(grad_block * grad_block)
    extra = jnp.zeros((2 * PAD - gain_rows % (2 * PAD), cols_here), jnp.float32).at[0, 0].set(square_part)
    packed = chip_then_y_sum(jnp.concatenate([part_proj, gain_block, extra], axis=0))
    proj_full = packed[:rank]
    square_shard = packed[rank + gain_rows, 0]
    gain_total = packed[rank:rank + gain_rows].reshape(-1)[:gain_len]
    proj_rows = lax.dynamic_slice_in_dim(proj_full, shard_pos * rank_rows, rank_rows, 0)

    refresh_part = lax.dot_general(
        grad_block, proj_full, (((1,), (1,)), ((), ())), precision=exact_mode
    )
    extra_r = jnp.zeros((PAD, rank), jnp.float32).at[0, 0].set(square_shard)
    packed_r = butterfly_sum(jnp.concatenate([refresh_part, extra_r], axis=0), "tensor")
    square_st = packed_r[rows_here, 0]
    refresh_rows = packed_r[:rows_here]
    frob_row = jnp.zeros((PAD, rank), jnp.float32).at[0, 0].set(jnp.sum(refresh_rows * refresh_rows))
    gathered = lax.all_gather(jnp.concatenate([refresh_rows, frob_row], 0), SHARD, axis=0, tiled=False)
    refreshed = gathered[:, :rows_here].reshape(shard_count * rows_here, rank)
    frob = jnp.sum(gathered[:, rows_here, 0])

    gain_own = lax.dynamic_slice_in_dim(gain_total, shard_pos * rows_here, rows_here, 0)
    square_local = square_st + jnp.sum(gain_total * gain_total)
    total_sq = butterfly_sum(jnp.full((PAD, 128), square_local, jnp.float32), "section")[0, 0]
    entry_count = float(lax.axis_size("section") * layer_count * (D * FF + D))
    clip = jnp.minimum(1.0, lax.rsqrt(total_sq / entry_count + clip_eps))

    first_new, second_new, direction = adam_direction(
        clip * proj_rows, first_moment[layer_index], second_moment[layer_index]
    )
    update_here = jnp.dot(
        basis_here, lax.all_gather(direction, SHARD, axis=0, tiled=True), precision=ns_mode
    )

    current = refreshed / jnp.sqrt(frob + ns_eps)
    for step_index in range(NS_STEPS - 1):
        current = coef_first * current + jnp.dot(current, mixer_of(current), precision=ns_mode)
    row_start = shard_pos * rows_here + tensor_pos * out_rows
    own = lax.dynamic_slice_in_dim(current, row_start, out_rows, 0)
    own = coef_first * own + jnp.dot(own, mixer_of(current), precision=ns_mode)

    gain_first_new, gain_second_new, gain_dir = adam_direction(
        clip * gain_own, gain_first[layer_index], gain_second[layer_index]
    )
    return (
        update_here[None],
        first_new[None],
        second_new[None],
        own[None],
        gain_dir[None],
        gain_first_new[None],
        gain_second_new[None],
    )


def solution(mesh):
    names = mesh.axis_names
    sizes = dict(mesh.shape)
    chip_y = sizes["shard"] // 2
    split_shape = []
    split_names = []
    for name in names:
        if name == "shard":
            split_shape += [chip_y, 2]
            split_names += ["chip_y", "core"]
        else:
            split_shape.append(sizes[name])
            split_names.append(name)
    split = jax.sharding.Mesh(mesh.devices.reshape(split_shape), tuple(split_names))
    placed = (
        P("section", SHARD, None),
        P("section", SHARD, "tensor"),
        P("section", SHARD, None),
        P("section", SHARD, "tensor"),
        P("section", SHARD, "tensor"),
        P("section", SHARD, None),
        P("section", SHARD),
        P("section", SHARD),
    )
    return jax.shard_map(
        shards,
        mesh=split,
        in_specs=placed,
        out_specs=(
            P("section", SHARD, "tensor"),
            P("section", SHARD, "tensor"),
            P("section", SHARD, "tensor"),
            P("section", SHARD + ("tensor",), None),
            P("section", SHARD),
            P("section", SHARD),
            P("section", SHARD),
        ),
        check_vma=False,
    )
```

```python
import jax
import jax.numpy as jnp
from jax import lax
from jax.sharding import PartitionSpec as P

D = 2048
FF = 8192
NS_STEPS = 5
STEP = 8


exact_mode = lax.Precision.HIGHEST
beta_one = 0.9
beta_two = 0.999
adam_eps = 1e-08
clip_eps = 1e-06
ns_eps = 1e-07
coef_first = 3.4445
coef_second = -4.775
coef_third = 2.0315
PAD = 8
SHARD = ("chip_y", "core")


def adam_direction(clipped, first_old, second_old):
    first_new = beta_one * first_old + (1.0 - beta_one) * clipped
    second_new = beta_two * second_old + (1.0 - beta_two) * clipped * clipped
    direction = (
        first_new
        / (1.0 - beta_one**STEP)
        / (jnp.sqrt(second_new / (1.0 - beta_two**STEP)) + adam_eps)
    )
    return (first_new, second_new, direction)


ns_mode = lax.Precision.HIGH


def mixer_of(current):
    gram = jnp.dot(current.T, current, precision=ns_mode)
    return coef_second * gram + coef_third * jnp.dot(gram, gram, precision=ns_mode)


def split3(x):
    hi = lax.reduce_precision(x, exponent_bits=8, mantissa_bits=7)
    rest = x - hi
    mid = lax.reduce_precision(rest, exponent_bits=8, mantissa_bits=7)
    lo = rest - mid
    return tuple(p.astype(jnp.bfloat16) for p in (hi, mid, lo))


def dot_split(lhs, rhs_pieces, dims):
    out = None
    for piece in rhs_pieces:
        term = lax.dot_general(lhs, piece, dims, preferred_element_type=jnp.float32)
        out = term if out is None else out + term
    return out


def butterfly_sum(x, axis):
    n = lax.axis_size(axis)
    k = 1
    while k < n:
        x = x + lax.ppermute(x, axis, [(i, i ^ k) for i in range(n)])
        k *= 2
    return x


def chip_then_y_sum(x):
    core = lax.axis_index("core")
    half = x.shape[0] // 2
    swap = [(0, 1), (1, 0)]
    mine = lax.dynamic_slice_in_dim(x, core * half, half, 0)
    theirs = lax.dynamic_slice_in_dim(x, (1 - core) * half, half, 0)
    mine = mine + lax.ppermute(theirs, "core", swap)
    mine = lax.psum(mine, "chip_y")
    other = lax.ppermute(mine, "core", swap)
    first = jnp.where(core == 0, mine, other)
    second = jnp.where(core == 0, other, mine)
    return jnp.concatenate([first, second], axis=0)


def shards(
    activations, out_grad, basis, first_moment, second_moment, gain_partial, gain_first, gain_second
):
    tensors = lax.axis_size("tensor")
    shard_count = lax.axis_size(SHARD)
    shard_pos = lax.axis_index(SHARD)
    tensor_pos = lax.axis_index("tensor")
    layer_count = activations.shape[0]
    rows_here = basis.shape[1]
    rank_rows = first_moment.shape[1]
    cols_here = out_grad.shape[2]
    rank = basis.shape[2]
    out_rows = rows_here // tensors
    layer_index = 0
    tokens_in = activations[layer_index]
    grads_out = out_grad[layer_index]
    basis_here = basis[layer_index]

    partial_grad = lax.dot_general(
        tokens_in, grads_out, (((0,), (0,)), ((), ())), preferred_element_type=jnp.float32
    )
    grad_block = lax.psum_scatter(partial_grad, SHARD, scatter_dimension=0, tiled=True)
    part_proj = jnp.dot(basis_here.T, grad_block, precision=exact_mode)
    gain_row = gain_partial[layer_index, 0]
    gain_len = gain_row.shape[0]
    gain_rows = -(-gain_len // cols_here)
    gain_block = jnp.pad(gain_row, (0, gain_rows * cols_here - gain_len)).reshape(gain_rows, cols_here)
    square_part = jnp.sum(grad_block * grad_block)
    extra = jnp.zeros((2 * PAD - gain_rows % (2 * PAD), cols_here), jnp.float32).at[0, 0].set(square_part)
    packed = chip_then_y_sum(jnp.concatenate([part_proj, gain_block, extra], axis=0))
    proj_full = packed[:rank]
    square_shard = packed[rank + gain_rows, 0]
    gain_total = packed[rank:rank + gain_rows].reshape(-1)[:gain_len]
    proj_rows = lax.dynamic_slice_in_dim(proj_full, shard_pos * rank_rows, rank_rows, 0)

    refresh_part = lax.dot_general(
        grad_block, proj_full, (((1,), (1,)), ((), ())), precision=exact_mode
    )
    extra_r = jnp.zeros((PAD, rank), jnp.float32).at[0, 0].set(square_shard)
    packed_r = butterfly_sum(jnp.concatenate([refresh_part, extra_r], axis=0), "tensor")
    square_st = packed_r[rows_here, 0]
    refresh_rows = packed_r[:rows_here]
    frob_row = jnp.zeros((PAD, rank), jnp.float32).at[0, 0].set(jnp.sum(refresh_rows * refresh_rows))
    gathered = lax.all_gather(jnp.concatenate([refresh_rows, frob_row], 0), SHARD, axis=0, tiled=False)
    refreshed = gathered[:, :rows_here].reshape(shard_count * rows_here, rank)
    frob = jnp.sum(gathered[:, rows_here, 0])

    gain_own = lax.dynamic_slice_in_dim(gain_total, shard_pos * rows_here, rows_here, 0)
    square_local = square_st + jnp.sum(gain_total * gain_total)
    total_sq = butterfly_sum(jnp.full((PAD, 128), square_local, jnp.float32), "section")[0, 0]
    entry_count = float(lax.axis_size("section") * layer_count * (D * FF + D))
    clip = jnp.minimum(1.0, lax.rsqrt(total_sq / entry_count + clip_eps))

    first_new, second_new, direction = adam_direction(
        clip * proj_rows, first_moment[layer_index], second_moment[layer_index]
    )
    direction_sent = direction + 0.0 * frob
    update_here = jnp.dot(
        basis_here, lax.all_gather(direction_sent, SHARD, axis=0, tiled=True), precision=ns_mode
    )

    current = refreshed / jnp.sqrt(frob + ns_eps)
    for step_index in range(NS_STEPS - 1):
        current = coef_first * current + jnp.dot(current, mixer_of(current), precision=ns_mode)
    row_start = shard_pos * rows_here + tensor_pos * out_rows
    own = lax.dynamic_slice_in_dim(current, row_start, out_rows, 0)
    own = coef_first * own + jnp.dot(own, mixer_of(current), precision=ns_mode)

    gain_first_new, gain_second_new, gain_dir = adam_direction(
        clip * gain_own, gain_first[layer_index], gain_second[layer_index]
    )
    return (
        update_here[None],
        first_new[None],
        second_new[None],
        own[None],
        gain_dir[None],
        gain_first_new[None],
        gain_second_new[None],
    )


def solution(mesh):
    names = mesh.axis_names
    sizes = dict(mesh.shape)
    chip_y = sizes["shard"] // 2
    split_shape = []
    split_names = []
    for name in names:
        if name == "shard":
            split_shape += [chip_y, 2]
            split_names += ["chip_y", "core"]
        else:
            split_shape.append(sizes[name])
            split_names.append(name)
    split = jax.sharding.Mesh(mesh.devices.reshape(split_shape), tuple(split_names))
    placed = (
        P("section", SHARD, None),
        P("section", SHARD, "tensor"),
        P("section", SHARD, None),
        P("section", SHARD, "tensor"),
        P("section", SHARD, "tensor"),
        P("section", SHARD, None),
        P("section", SHARD),
        P("section", SHARD),
    )
    return jax.shard_map(
        shards,
        mesh=split,
        in_specs=placed,
        out_specs=(
            P("section", SHARD, "tensor"),
            P("section", SHARD, "tensor"),
            P("section", SHARD, "tensor"),
            P("section", SHARD + ("tensor",), None),
            P("section", SHARD),
            P("section", SHARD),
            P("section", SHARD),
        ),
        check_vma=False,
    )
```

```python
import jax
import jax.numpy as jnp
from jax import lax
from jax.sharding import PartitionSpec as P

D = 2048
FF = 8192
NS_STEPS = 5
STEP = 8


exact_mode = lax.Precision.HIGHEST
beta_one = 0.9
beta_two = 0.999
adam_eps = 1e-08
clip_eps = 1e-06
ns_eps = 1e-07
coef_first = 3.4445
coef_second = -4.775
coef_third = 2.0315
PAD = 8
SHARD = ("chip_y", "core")


def adam_direction(clipped, first_old, second_old):
    first_new = beta_one * first_old + (1.0 - beta_one) * clipped
    second_new = beta_two * second_old + (1.0 - beta_two) * clipped * clipped
    direction = (
        first_new
        / (1.0 - beta_one**STEP)
        / (jnp.sqrt(second_new / (1.0 - beta_two**STEP)) + adam_eps)
    )
    return (first_new, second_new, direction)


ns_mode = lax.Precision.HIGH


def mixer_of(current):
    gram = jnp.dot(current.T, current, precision=ns_mode)
    return coef_second * gram + coef_third * jnp.dot(gram, gram, precision=ns_mode)


def split3(x):
    hi = lax.reduce_precision(x, exponent_bits=8, mantissa_bits=7)
    rest = x - hi
    mid = lax.reduce_precision(rest, exponent_bits=8, mantissa_bits=7)
    lo = rest - mid
    return tuple(p.astype(jnp.bfloat16) for p in (hi, mid, lo))


def dot_split(lhs, rhs_pieces, dims):
    out = None
    for piece in rhs_pieces:
        term = lax.dot_general(lhs, piece, dims, preferred_element_type=jnp.float32)
        out = term if out is None else out + term
    return out


def butterfly_sum(x, axis):
    n = lax.axis_size(axis)
    k = 1
    while k < n:
        x = x + lax.ppermute(x, axis, [(i, i ^ k) for i in range(n)])
        k *= 2
    return x


def chip_then_y_sum(x):
    core = lax.axis_index("core")
    half = x.shape[0] // 2
    swap = [(0, 1), (1, 0)]
    mine = lax.dynamic_slice_in_dim(x, core * half, half, 0)
    theirs = lax.dynamic_slice_in_dim(x, (1 - core) * half, half, 0)
    mine = mine + lax.ppermute(theirs, "core", swap)
    mine = lax.psum(mine, "chip_y")
    other = lax.ppermute(mine, "core", swap)
    first = jnp.where(core == 0, mine, other)
    second = jnp.where(core == 0, other, mine)
    return jnp.concatenate([first, second], axis=0)


def shards(
    activations, out_grad, basis, first_moment, second_moment, gain_partial, gain_first, gain_second
):
    tensors = lax.axis_size("tensor")
    shard_count = lax.axis_size(SHARD)
    shard_pos = lax.axis_index(SHARD)
    tensor_pos = lax.axis_index("tensor")
    layer_count = activations.shape[0]
    rows_here = basis.shape[1]
    rank_rows = first_moment.shape[1]
    cols_here = out_grad.shape[2]
    rank = basis.shape[2]
    out_rows = rows_here // tensors
    layer_index = 0
    tokens_in = activations[layer_index]
    grads_out = out_grad[layer_index]
    basis_here = basis[layer_index]

    partial_grad = lax.dot_general(
        tokens_in, grads_out, (((0,), (0,)), ((), ())), preferred_element_type=jnp.float32
    )
    grad_block = lax.psum_scatter(partial_grad, SHARD, scatter_dimension=0, tiled=True)
    part_proj = jnp.dot(basis_here.T, grad_block, precision=exact_mode)
    gain_row = gain_partial[layer_index, 0]
    gain_len = gain_row.shape[0]
    gain_rows = -(-gain_len // cols_here)
    gain_block = jnp.pad(gain_row, (0, gain_rows * cols_here - gain_len)).reshape(gain_rows, cols_here)
    square_part = jnp.sum(grad_block * grad_block)
    extra = jnp.zeros((2 * PAD - gain_rows % (2 * PAD), cols_here), jnp.float32).at[0, 0].set(square_part)
    packed = chip_then_y_sum(jnp.concatenate([part_proj, gain_block, extra], axis=0))
    proj_full = packed[:rank]
    square_shard = packed[rank + gain_rows, 0]
    gain_total = packed[rank:rank + gain_rows].reshape(-1)[:gain_len]
    proj_rows = lax.dynamic_slice_in_dim(proj_full, shard_pos * rank_rows, rank_rows, 0)

    refresh_part = lax.dot_general(
        grad_block, proj_full, (((1,), (1,)), ((), ())), precision=exact_mode
    )
    extra_r = jnp.zeros((PAD, rank), jnp.float32).at[0, 0].set(square_shard)
    packed_r = butterfly_sum(jnp.concatenate([refresh_part, extra_r], axis=0), "tensor")
    square_st = packed_r[rows_here, 0]
    refreshed = lax.all_gather(packed_r[:rows_here], SHARD, axis=0, tiled=True)

    gain_own = lax.dynamic_slice_in_dim(gain_total, shard_pos * rows_here, rows_here, 0)
    square_local = square_st + jnp.sum(gain_total * gain_total)
    total_sq = butterfly_sum(jnp.full((PAD, 128), square_local, jnp.float32), "section")[0, 0]
    entry_count = float(lax.axis_size("section") * layer_count * (D * FF + D))
    clip = jnp.minimum(1.0, lax.rsqrt(total_sq / entry_count + clip_eps))

    first_new, second_new, direction = adam_direction(
        clip * proj_rows, first_moment[layer_index], second_moment[layer_index]
    )
    update_here = jnp.dot(
        basis_here, lax.all_gather(direction, SHARD, axis=0, tiled=True), precision=ns_mode
    )

    current = refreshed / jnp.sqrt(jnp.sum(refreshed * refreshed) + ns_eps)
    for step_index in range(NS_STEPS - 1):
        current = coef_first * current + jnp.dot(current, mixer_of(current), precision=ns_mode)
    row_start = shard_pos * rows_here + tensor_pos * out_rows
    own = lax.dynamic_slice_in_dim(current, row_start, out_rows, 0)
    own = coef_first * own + jnp.dot(own, mixer_of(current), precision=ns_mode)

    gain_first_new, gain_second_new, gain_dir = adam_direction(
        clip * gain_own, gain_first[layer_index], gain_second[layer_index]
    )
    return (
        update_here[None],
        first_new[None],
        second_new[None],
        own[None],
        gain_dir[None],
        gain_first_new[None],
        gain_second_new[None],
    )


def solution(mesh):
    names = mesh.axis_names
    sizes = dict(mesh.shape)
    chip_y = sizes["shard"] // 2
    split_shape = []
    split_names = []
    for name in names:
        if name == "shard":
            split_shape += [chip_y, 2]
            split_names += ["chip_y", "core"]
        else:
            split_shape.append(sizes[name])
            split_names.append(name)
    split = jax.sharding.Mesh(mesh.devices.reshape(split_shape), tuple(split_names))
    placed = (
        P("section", SHARD, None),
        P("section", SHARD, "tensor"),
        P("section", SHARD, None),
        P("section", SHARD, "tensor"),
        P("section", SHARD, "tensor"),
        P("section", SHARD, None),
        P("section", SHARD),
        P("section", SHARD),
    )
    return jax.shard_map(
        shards,
        mesh=split,
        in_specs=placed,
        out_specs=(
            P("section", SHARD, "tensor"),
            P("section", SHARD, "tensor"),
            P("section", SHARD, "tensor"),
            P("section", SHARD + ("tensor",), None),
            P("section", SHARD),
            P("section", SHARD),
            P("section", SHARD),
        ),
        check_vma=False,
    )
```
